256 devices in a mesh: rad: 8 (over z_hi, core), azi: 32 (over y, x, z_lo).
Axes of the slice: x: 4, y: 4, z: 8 (z_hi: 4, z_lo: 2; z = z_hi * 2 + z_lo), core: 2. Of those that a mesh axis runs over, the one named last changes fastest.
Arguments:
- gas_state: float32 [4, 16, 512, 1024], P(None, None, 'azi', 'rad'), may hold values from -6 to 6
- sound_sq: float32 [16, 512, 1024], P(None, 'azi', 'rad'), may hold values from 0.5 to 2
- offsets: int32 [1024], P('rad'), may hold values from 0 to 511
Outputs:
- final_state: float32 [4, 16, 512, 1024], P(None, None, 'azi', 'rad')
The draws below stay inside these ranges and needn't reach their ends.
All inputs are finite; a program needn't handle non-finite values.
Results may differ from the reference program's by a relative error of at most 0.00002.
Values sent between devices are 32-bit elements; how exact they have to be, the bound alone decides.
No kernel may reach another device: no remote copies, remote signals or barrier semaphores. Data moves between devices by JAX's collectives and lax.ppermute only.
A program may use at most 64 MiB of HBM per device.

```python
import math
import jax
import jax.numpy as jnp
from jax import lax

NZ = 16
ORDER = 4
STEPS = 2
NR = 1024
NA = 512


def with_ends(drawn, own_key, least, largest):
    dims = drawn.shape
    index_at = [jax.random.randint(jax.random.fold_in(own_key, axis), (), 0, dims[axis]) for axis in range(len(dims))]
    drawn = drawn.at[tuple(index_at)].set(least)
    longest = dims.index(max(dims))
    index_at[longest] = (index_at[longest] + 1) % dims[longest]
    return drawn.at[tuple(index_at)].set(largest)


def levels(own_key, extent, cuts, smallest, top_value):
    level = 1.0
    for dim, shards_of in cuts:
        steps = jax.random.uniform(jax.random.fold_in(jax.random.fold_in(own_key, 6), dim), (shards_of,), jnp.float32, smallest / len(cuts), top_value / len(cuts))
        level = level * jnp.repeat(jnp.exp(steps), extent[dim] // shards_of).reshape((-1,) + (1,) * (len(extent) - 1 - dim))
    return level


def noise(rng, shape, scale, limit, shards=(), kind=jnp.bfloat16):
    values = jax.random.normal(rng, shape, jnp.float32) * scale
    if len(shards) > 0:
        values = levels(rng, shape, shards, -0.22, 0.18) * values
    return jnp.clip(values, min=-limit, max=limit).astype(kind)


def setup_inputs(seed: int = 0) -> dict:
    seeds = jax.random.split(jax.random.key(seed), 4)
    return {
        "gas_state": noise(seeds[0], (4, NZ, NA, NR), 1.0, 6.0, ((2, 32), (3, 8)), jnp.float32),
        "sound_sq": jnp.clip(jnp.exp(math.log(2.0) - 1.3862944 * jax.random.uniform(seeds[1], (NZ, NA, NR), jnp.float32) ** levels(seeds[1], (NZ, NA, NR), ((1, 32), (2, 8)), -0.2, 0.2)), 0.5, 2.0),
        "offsets": with_ends(jax.random.randint(seeds[2], (NR,), 0, NA), jax.random.fold_in(seeds[2], 1), 0, NA - 1).astype(jnp.int32),
    }


TIME_STEP = 0.5
ANGULAR_RATE = 1.0
SHEAR_RATE = 1.5


def window(values, start, length, which_dim):
    return lax.slice_in_dim(values, start, start + length, axis=which_dim)


def diff_along(values, which_dim):
    length = values.shape[which_dim] - 4
    return (8.0 * (window(values, 3, length, which_dim) - window(values, 1, length, which_dim))
            - (window(values, 4, length, which_dim) - window(values, 0, length, which_dim))) / 12.0


def diff_vertical(values):
    return (8.0 * (jnp.roll(values, -1, 0) - jnp.roll(values, 1, 0))
            - (jnp.roll(values, -2, 0) - jnp.roll(values, 2, 0))) / 12.0


def inner_part(values):
    return values[:, 2:-2, 2:-2]


def operator_core(pressure, radial_flow, azimuth_flow, vertical_flow):
    density_rate = -(diff_along(radial_flow[:, 2:-2, :], 2) + diff_along(azimuth_flow[:, :, 2:-2], 1)
                     + diff_vertical(inner_part(vertical_flow)))
    radial_rate = -diff_along(pressure[:, 2:-2, :], 2) + 2.0 * ANGULAR_RATE * inner_part(azimuth_flow)
    azimuth_rate = -diff_along(pressure[:, :, 2:-2], 1) - (2.0 - SHEAR_RATE) * ANGULAR_RATE * inner_part(radial_flow)
    vertical_rate = -diff_vertical(inner_part(pressure))
    return jnp.stack([density_rate, radial_rate, azimuth_rate, vertical_rate])


def pad_field(values):
    wrapped = jnp.pad(values, ((0, 0), (2, 2), (0, 0)), mode="wrap")
    return jnp.pad(wrapped, ((0, 0), (0, 0), (2, 2)))


def roll_row(column, shift_cells):
    return jnp.roll(column, shift_cells, axis=2)


def shear_rows(values, offsets):
    return jax.vmap(roll_row, in_axes=(3, 0), out_axes=3)(values, offsets)


def reference(gas_state, sound_sq, offsets):
    state = gas_state
    for timestep in range(STEPS):
        running = state
        series = state
        for degree in range(1, ORDER + 1):
            rates = operator_core(pad_field(sound_sq * series[0]), pad_field(series[1]),
                                  pad_field(series[2]), pad_field(series[3]))
            series = (TIME_STEP / degree) * rates
            running = running + series
        state = shear_rows(running, offsets)
    return state
```

```python
import jax
import jax.numpy as jnp
from jax import lax
from jax.sharding import PartitionSpec as P

ORDER = 4
STEPS = 2


TIME_STEP = 0.5
ANGULAR_RATE = 1.0
SHEAR_RATE = 1.5


def ring(axis, by):
    count = lax.axis_size(axis)
    return [(i, (i + by) % count) for i in range(count)]


def window(values, start, length, which_dim):
    return lax.slice_in_dim(values, start, start + length, axis=which_dim)


def diff_along(values, which_dim):
    length = values.shape[which_dim] - 4
    return (
        8.0 * (window(values, 3, length, which_dim) - window(values, 1, length, which_dim))
        - (window(values, 4, length, which_dim) - window(values, 0, length, which_dim))
    ) / 12.0


def diff_vertical(values):
    return (
        8.0 * (jnp.roll(values, -1, 0) - jnp.roll(values, 1, 0))
        - (jnp.roll(values, -2, 0) - jnp.roll(values, 2, 0))
    ) / 12.0


def halos(pressure, radial_flow, azimuth_flow):
    rad_cells = jnp.stack([pressure, radial_flow])
    azi_cells = jnp.stack([pressure, azimuth_flow])
    rows = rad_cells.shape[3]
    cells = azi_cells.shape[2]
    rad_tail = lax.ppermute(rad_cells[..., rows - 2:], "rad", ring("rad", 1))
    rad_head = lax.ppermute(rad_cells[..., :2], "rad", ring("rad", -1))
    azi_tail = lax.ppermute(azi_cells[:, :, cells - 2:, :], "azi", ring("azi", 1))
    azi_head = lax.ppermute(azi_cells[:, :, :2, :], "azi", ring("azi", -1))
    rad_index = lax.axis_index("rad")
    rad_tail = jnp.where(rad_index == 0, 0.0, rad_tail)
    rad_head = jnp.where(rad_index == lax.axis_size("rad") - 1, 0.0, rad_head)
    rad_padded = jnp.concatenate([rad_tail, rad_cells, rad_head], axis=3)
    azi_padded = jnp.concatenate([azi_tail, azi_cells, azi_head], axis=2)
    return rad_padded, azi_padded


def operator(series, sound_sq):
    pressure = sound_sq * series[0]
    radial_flow, azimuth_flow, vertical_flow = series[1], series[2], series[3]
    rad_padded, azi_padded = halos(pressure, radial_flow, azimuth_flow)
    density_rate = -(
        diff_along(rad_padded[1], 2) + diff_along(azi_padded[1], 1) + diff_vertical(vertical_flow)
    )
    radial_rate = -diff_along(rad_padded[0], 2) + 2.0 * ANGULAR_RATE * azimuth_flow
    azimuth_rate = -diff_along(azi_padded[0], 1) - (2.0 - SHEAR_RATE) * ANGULAR_RATE * radial_flow
    vertical_rate = -diff_vertical(pressure)
    return jnp.stack([density_rate, radial_rate, azimuth_rate, vertical_rate])


def taylor(state, sound_sq):
    running = state
    series = state
    for degree in range(1, ORDER + 1):
        series = TIME_STEP / degree * operator(series, sound_sq)
        running = running + series
    return running


def remap(state, offsets):
    fields, depth, cells, rows = state.shape
    planes = state.reshape(fields * depth, cells, rows)
    whole = lax.all_to_all(planes, "azi", 0, 1, tiled=True)
    total = whole.shape[1]
    for bit_pos in range((total - 1).bit_length()):
        chosen = (offsets >> bit_pos) & 1 == 1
        whole = jnp.where(chosen[None, None, :], jnp.roll(whole, 1 << bit_pos, axis=1), whole)
    planes = lax.all_to_all(whole, "azi", 1, 0, tiled=True)
    return planes.reshape(fields, depth, cells, rows)


def per_device(gas_state, sound_sq, offsets):
    state = gas_state
    for timestep in range(STEPS):
        running = taylor(state, sound_sq)
        state = remap(running, offsets)
    return state


def solution(mesh):
    in_specs = (P(None, None, "azi", "rad"), P(None, "azi", "rad"), P("rad"))
    out_specs = P(None, None, "azi", "rad")
    return jax.shard_map(
        per_device, mesh=mesh, in_specs=in_specs, out_specs=out_specs, check_vma=False
    )
```

```python
import jax
import jax.numpy as jnp
from jax import lax
from jax.sharding import PartitionSpec as P

ORDER = 4
STEPS = 2


TIME_STEP = 0.5
ANGULAR_RATE = 1.0
SHEAR_RATE = 1.5


def ring(axis, by):
    count = lax.axis_size(axis)
    return [(i, (i + by) % count) for i in range(count)]


def window(values, start, length, which_dim):
    return lax.slice_in_dim(values, start, start + length, axis=which_dim)


def diff_along(values, which_dim):
    length = values.shape[which_dim] - 4
    return (
        8.0 * (window(values, 3, length, which_dim) - window(values, 1, length, which_dim))
        - (window(values, 4, length, which_dim) - window(values, 0, length, which_dim))
    ) / 12.0


def diff_vertical(values):
    return (
        8.0 * (jnp.roll(values, -1, 0) - jnp.roll(values, 1, 0))
        - (jnp.roll(values, -2, 0) - jnp.roll(values, 2, 0))
    ) / 12.0


def neighbour(cells, rad_by, azi_by):
    rads, azis = lax.axis_size("rad"), lax.axis_size("azi")
    pairs = [
        (r * azis + a, ((r + rad_by) % rads) * azis + (a + azi_by) % azis)
        for r in range(rads)
        for a in range(azis)
    ]
    return lax.ppermute(cells, ("rad", "azi"), pairs)


def extended(cells, depth):
    rows = cells.shape[3]
    count = cells.shape[2]
    low_a, high_a = slice(count - depth, count), slice(0, depth)
    low_r, high_r = slice(rows - depth, rows), slice(0, depth)
    band = []
    for azi_by, azi_part in ((1, low_a), (0, slice(None)), (-1, high_a)):
        pieces = []
        for rad_by, rad_part in ((1, low_r), (0, slice(None)), (-1, high_r)):
            piece = cells[:, :, azi_part, rad_part]
            if rad_by or azi_by:
                piece = neighbour(piece, rad_by, azi_by)
            pieces.append(piece)
        band.append(jnp.concatenate(pieces, axis=3))
    return jnp.concatenate(band, axis=2)


def inside_rows(start, extent, depth, row_count):
    global_row = (
        lax.axis_index("rad") * row_count - depth + start + jnp.arange(extent, dtype=jnp.int32)
    )
    return (global_row >= 0) & (global_row < row_count * lax.axis_size("rad"))


def operator_core(pressure, radial_flow, azimuth_flow, vertical_flow):
    density_rate = -(
        diff_along(radial_flow[:, 2:-2, :], 2)
        + diff_along(azimuth_flow[:, :, 2:-2], 1)
        + diff_vertical(inner_part(vertical_flow))
    )
    radial_rate = -diff_along(pressure[:, 2:-2, :], 2) + 2.0 * ANGULAR_RATE * inner_part(
        azimuth_flow
    )
    azimuth_rate = -diff_along(pressure[:, :, 2:-2], 1) - (
        2.0 - SHEAR_RATE
    ) * ANGULAR_RATE * inner_part(radial_flow)
    vertical_rate = -diff_vertical(inner_part(pressure))
    return jnp.stack([density_rate, radial_rate, azimuth_rate, vertical_rate])


def inner_part(values):
    return values[:, 2:-2, 2:-2]


def taylor(wide_state, wide_sound, depth, cells, row_count):
    keep = inside_rows(0, wide_state.shape[3], depth, row_count)
    series = jnp.where(keep, wide_state, 0.0)
    running = wide_state[:, :, depth:depth + cells, depth:depth + row_count]
    for degree in range(1, ORDER + 1):
        edge = 2 * (degree - 1)
        sound = wide_sound[:, edge:wide_sound.shape[1] - edge, edge:wide_sound.shape[2] - edge]
        series = TIME_STEP / degree * operator_core(
            sound * series[0], series[1], series[2], series[3]
        )
        margin = depth - 2 * degree
        keep = inside_rows(2 * degree, series.shape[3], depth, row_count)
        series = jnp.where(keep, series, 0.0)
        running = running + series[:, :, margin:margin + cells, margin:margin + row_count]
    return running


def remap(state, offsets):
    fields, depth, cells, rows = state.shape
    planes = state.reshape(fields * depth, cells, rows)
    whole = lax.all_to_all(planes, "azi", 0, 1, tiled=True)
    total = whole.shape[1]
    for bit_pos in range((total - 1).bit_length()):
        chosen = (offsets >> bit_pos) & 1 == 1
        whole = jnp.where(chosen[None, None, :], jnp.roll(whole, 1 << bit_pos, axis=1), whole)
    planes = lax.all_to_all(whole, "azi", 1, 0, tiled=True)
    return planes.reshape(fields, depth, cells, rows)


def per_device(gas_state, sound_sq, offsets):
    depth = 2 * ORDER
    cells, row_count = gas_state.shape[2], gas_state.shape[3]
    wide = extended(jnp.concatenate([gas_state, sound_sq[None]]), depth)
    wide_state, wide_sound = wide[:4], wide[4]
    for timestep in range(STEPS):
        if timestep:
            wide_state = extended(state, depth)
        running = taylor(wide_state, wide_sound, depth, cells, row_count)
        state = remap(running, offsets)
    return state


def solution(mesh):
    in_specs = (P(None, None, "azi", "rad"), P(None, "azi", "rad"), P("rad"))
    out_specs = P(None, None, "azi", "rad")
    return jax.shard_map(
        per_device, mesh=mesh, in_specs=in_specs, out_specs=out_specs, check_vma=False
    )
```

```python
import jax
import jax.numpy as jnp
from jax import lax
from jax.sharding import PartitionSpec as P

ORDER = 4
STEPS = 2


TIME_STEP = 0.5
ANGULAR_RATE = 1.0
SHEAR_RATE = 1.5


def ring(axis, by):
    count = lax.axis_size(axis)
    return [(i, (i + by) % count) for i in range(count)]


def window(values, start, length, which_dim):
    return lax.slice_in_dim(values, start, start + length, axis=which_dim)


def diff_along(values, which_dim):
    length = values.shape[which_dim] - 4
    return (
        8.0 * (window(values, 3, length, which_dim) - window(values, 1, length, which_dim))
        - (window(values, 4, length, which_dim) - window(values, 0, length, which_dim))
    ) / 12.0


def diff_vertical(values):
    return (
        8.0 * (jnp.roll(values, -1, 0) - jnp.roll(values, 1, 0))
        - (jnp.roll(values, -2, 0) - jnp.roll(values, 2, 0))
    ) / 12.0


def extended(cells, depth):
    count = cells.shape[2]
    cells = jnp.concatenate(
        [
            lax.ppermute(cells[:, :, count - depth:, :], "azi", ring("azi", 1)),
            cells,
            lax.ppermute(cells[:, :, :depth, :], "azi", ring("azi", -1)),
        ],
        axis=2,
    )
    rows = cells.shape[3]
    return jnp.concatenate(
        [
            lax.ppermute(cells[..., rows - depth:], "rad", ring("rad", 1)),
            cells,
            lax.ppermute(cells[..., :depth], "rad", ring("rad", -1)),
        ],
        axis=3,
    )


def inside_rows(start, extent, depth, row_count):
    global_row = (
        lax.axis_index("rad") * row_count - depth + start + jnp.arange(extent, dtype=jnp.int32)
    )
    return (global_row >= 0) & (global_row < row_count * lax.axis_size("rad"))


def operator_core(pressure, radial_flow, azimuth_flow, vertical_flow):
    density_rate = -(
        diff_along(radial_flow[:, 2:-2, :], 2)
        + diff_along(azimuth_flow[:, :, 2:-2], 1)
        + diff_vertical(inner_part(vertical_flow))
    )
    radial_rate = -diff_along(pressure[:, 2:-2, :], 2) + 2.0 * ANGULAR_RATE * inner_part(
        azimuth_flow
    )
    azimuth_rate = -diff_along(pressure[:, :, 2:-2], 1) - (
        2.0 - SHEAR_RATE
    ) * ANGULAR_RATE * inner_part(radial_flow)
    vertical_rate = -diff_vertical(inner_part(pressure))
    return jnp.stack([density_rate, radial_rate, azimuth_rate, vertical_rate])


def inner_part(values):
    return values[:, 2:-2, 2:-2]


def taylor(wide_state, wide_sound, depth, cells, row_count):
    keep = inside_rows(0, wide_state.shape[3], depth, row_count)
    series = jnp.where(keep, wide_state, 0.0)
    running = wide_state[:, :, depth:depth + cells, depth:depth + row_count]
    for degree in range(1, ORDER + 1):
        edge = 2 * (degree - 1)
        sound = wide_sound[:, edge:wide_sound.shape[1] - edge, edge:wide_sound.shape[2] - edge]
        series = TIME_STEP / degree * operator_core(
            sound * series[0], series[1], series[2], series[3]
        )
        margin = depth - 2 * degree
        keep = inside_rows(2 * degree, series.shape[3], depth, row_count)
        series = jnp.where(keep, series, 0.0)
        running = running + series[:, :, margin:margin + cells, margin:margin + row_count]
    return running


def remap(state, offsets):
    fields, depth, cells, rows = state.shape
    planes = state.reshape(fields * depth, cells, rows)
    whole = lax.all_to_all(planes, "azi", 0, 1, tiled=True)
    total = whole.shape[1]
    for bit_pos in range((total - 1).bit_length()):
        chosen = (offsets >> bit_pos) & 1 == 1
        whole = jnp.where(chosen[None, None, :], jnp.roll(whole, 1 << bit_pos, axis=1), whole)
    planes = lax.all_to_all(whole, "azi", 1, 0, tiled=True)
    return planes.reshape(fields, depth, cells, rows)


def per_device(gas_state, sound_sq, offsets):
    depth = 2 * ORDER
    cells, row_count = gas_state.shape[2], gas_state.shape[3]
    wide = extended(jnp.concatenate([gas_state, sound_sq[None]]), depth)
    wide_state, wide_sound = wide[:4], wide[4]
    for timestep in range(STEPS):
        if timestep:
            wide_state = extended(state, depth)
        running = taylor(wide_state, wide_sound, depth, cells, row_count)
        state = remap(running, offsets)
    return state


def solution(mesh):
    in_specs = (P(None, None, "azi", "rad"), P(None, "azi", "rad"), P("rad"))
    out_specs = P(None, None, "azi", "rad")
    return jax.shard_map(
        per_device, mesh=mesh, in_specs=in_specs, out_specs=out_specs, check_vma=False
    )
```

```python
import jax
import jax.numpy as jnp
from jax import lax
from jax.sharding import PartitionSpec as P

ORDER = 4
STEPS = 2


TIME_STEP = 0.5
ANGULAR_RATE = 1.0
SHEAR_RATE = 1.5


def ring(axis, by):
    count = lax.axis_size(axis)
    return [(i, (i + by) % count) for i in range(count)]


def window(values, start, length, which_dim):
    return lax.slice_in_dim(values, start, start + length, axis=which_dim)


def diff_along(values, which_dim):
    length = values.shape[which_dim] - 4
    return (
        8.0 * (window(values, 3, length, which_dim) - window(values, 1, length, which_dim))
        - (window(values, 4, length, which_dim) - window(values, 0, length, which_dim))
    ) / 12.0


def diff_vertical(values):
    return (
        8.0 * (jnp.roll(values, -1, 0) - jnp.roll(values, 1, 0))
        - (jnp.roll(values, -2, 0) - jnp.roll(values, 2, 0))
    ) / 12.0


def azimuthal_halos(cells, depth):
    count = cells.shape[2]
    return jnp.concatenate(
        [
            lax.ppermute(cells[:, :, count - depth:, :], "azi", ring("azi", 1)),
            cells,
            lax.ppermute(cells[:, :, :depth, :], "azi", ring("azi", -1)),
        ],
        axis=2,
    )


def radial_halos(cells, depth):
    rows = cells.shape[3]
    return jnp.concatenate(
        [
            lax.ppermute(cells[..., rows - depth:], "rad", ring("rad", 1)),
            cells,
            lax.ppermute(cells[..., :depth], "rad", ring("rad", -1)),
        ],
        axis=3,
    )


def inside_rows(start, extent, depth, row_count):
    global_row = (
        lax.axis_index("rad") * row_count - depth + start + jnp.arange(extent, dtype=jnp.int32)
    )
    return (global_row >= 0) & (global_row < row_count * lax.axis_size("rad"))


def inner_part(values):
    return values[:, 2:-2, 2:-2]


def operator_core(pressure, radial_flow, azimuth_flow, vertical_flow):
    density_rate = -(
        diff_along(radial_flow[:, 2:-2, :], 2)
        + diff_along(azimuth_flow[:, :, 2:-2], 1)
        + diff_vertical(inner_part(vertical_flow))
    )
    radial_rate = -diff_along(pressure[:, 2:-2, :], 2) + 2.0 * ANGULAR_RATE * inner_part(
        azimuth_flow
    )
    azimuth_rate = -diff_along(pressure[:, :, 2:-2], 1) - (
        2.0 - SHEAR_RATE
    ) * ANGULAR_RATE * inner_part(radial_flow)
    vertical_rate = -diff_vertical(inner_part(pressure))
    return density_rate, radial_rate, azimuth_rate, vertical_rate


def taylor(wide_state, wide_sound, depth, cells, row_count):
    keep = inside_rows(0, wide_state.shape[3], depth, row_count)
    series = tuple(jnp.where(keep, field, 0.0) for field in wide_state)
    running = tuple(field[:, depth:depth + cells, depth:depth + row_count] for field in wide_state)
    for degree in range(1, ORDER + 1):
        edge = 2 * (degree - 1)
        sound = wide_sound[:, edge:wide_sound.shape[1] - edge, edge:wide_sound.shape[2] - edge]
        rates = operator_core(sound * series[0], series[1], series[2], series[3])
        margin = depth - 2 * degree
        keep = inside_rows(2 * degree, rates[0].shape[2], depth, row_count)
        series = tuple(jnp.where(keep, TIME_STEP / degree * rate, 0.0) for rate in rates)
        running = tuple(
            total + field[:, margin:margin + cells, margin:margin + row_count]
            for total, field in zip(running, series)
        )
    return jnp.stack(running)


def remap(state, offsets, depth):
    fields, levels, cells, rows = state.shape
    planes = state.reshape(fields * levels, cells, rows)
    whole = lax.all_to_all(planes, "azi", 0, 1, tiled=True)
    total = whole.shape[1]
    for bit_pos in range((total - 1).bit_length()):
        chosen = (offsets >> bit_pos) & 1 == 1
        whole = jnp.where(chosen[None, None, :], jnp.roll(whole, 1 << bit_pos, axis=1), whole)
    if depth == 0:
        planes = lax.all_to_all(whole, "azi", 1, 0, tiled=True)
        return planes.reshape(fields, levels, cells, rows)
    peers = total // cells
    padded = jnp.concatenate([whole[:, total - depth:], whole, whole[:, :cells - depth]], axis=1)
    blocks = padded.reshape(padded.shape[0], peers + 1, cells, rows)
    windows = jnp.concatenate([blocks[:, :peers], blocks[:, 1:, :2 * depth]], axis=2)
    windows = jnp.moveaxis(windows, 1, 0)
    planes = lax.all_to_all(windows, "azi", 0, 1, tiled=True)
    return planes.reshape(fields, levels, cells + 2 * depth, rows)


def per_device(gas_state, sound_sq, offsets):
    depth = 2 * ORDER
    cells, row_count = gas_state.shape[2], gas_state.shape[3]
    wide = radial_halos(azimuthal_halos(jnp.concatenate([gas_state, sound_sq[None]]), depth), depth)
    wide_state, wide_sound = wide[:4], wide[4]
    for timestep in range(STEPS):
        running = taylor(wide_state, wide_sound, depth, cells, row_count)
        last = timestep == STEPS - 1
        state = remap(running, offsets, 0 if last else depth)
        if not last:
            wide_state = radial_halos(state, depth)
    return state


def solution(mesh):
    in_specs = (P(None, None, "azi", "rad"), P(None, "azi", "rad"), P("rad"))
    out_specs = P(None, None, "azi", "rad")
    return jax.shard_map(
        per_device, mesh=mesh, in_specs=in_specs, out_specs=out_specs, check_vma=False
    )
```

```python
import jax
import jax.numpy as jnp
from jax import lax
from jax.sharding import PartitionSpec as P

ORDER = 4
STEPS = 2


TIME_STEP = 0.5
ANGULAR_RATE = 1.0
SHEAR_RATE = 1.5


def ring(axis, by):
    count = lax.axis_size(axis)
    return [(i, (i + by) % count) for i in range(count)]


def window(values, start, length, which_dim):
    return lax.slice_in_dim(values, start, start + length, axis=which_dim)


def diff_along(values, which_dim):
    length = values.shape[which_dim] - 4
    return (
        8.0 * (window(values, 3, length, which_dim) - window(values, 1, length, which_dim))
        - (window(values, 4, length, which_dim) - window(values, 0, length, which_dim))
    ) / 12.0


def diff_vertical(values):
    return (
        8.0 * (jnp.roll(values, -1, 0) - jnp.roll(values, 1, 0))
        - (jnp.roll(values, -2, 0) - jnp.roll(values, 2, 0))
    ) / 12.0


def extended(cells, depth):
    count = cells.shape[2]
    cells = jnp.concatenate(
        [
            lax.ppermute(cells[:, :, count - depth:, :], "azi", ring("azi", 1)),
            cells,
            lax.ppermute(cells[:, :, :depth, :], "azi", ring("azi", -1)),
        ],
        axis=2,
    )
    rows = cells.shape[3]
    return jnp.concatenate(
        [
            lax.ppermute(cells[..., rows - depth:], "rad", ring("rad", 1)),
            cells,
            lax.ppermute(cells[..., :depth], "rad", ring("rad", -1)),
        ],
        axis=3,
    )


def inside_rows(start, extent, depth, row_count):
    global_row = (
        lax.axis_index("rad") * row_count - depth + start + jnp.arange(extent, dtype=jnp.int32)
    )
    return (global_row >= 0) & (global_row < row_count * lax.axis_size("rad"))


def operator_core(pressure, radial_flow, azimuth_flow, vertical_flow):
    density_rate = -(
        diff_along(radial_flow[:, 2:-2, :], 2)
        + diff_along(azimuth_flow[:, :, 2:-2], 1)
        + diff_vertical(inner_part(vertical_flow))
    )
    radial_rate = -diff_along(pressure[:, 2:-2, :], 2) + 2.0 * ANGULAR_RATE * inner_part(
        azimuth_flow
    )
    azimuth_rate = -diff_along(pressure[:, :, 2:-2], 1) - (
        2.0 - SHEAR_RATE
    ) * ANGULAR_RATE * inner_part(radial_flow)
    vertical_rate = -diff_vertical(inner_part(pressure))
    return jnp.stack([density_rate, radial_rate, azimuth_rate, vertical_rate])


def inner_part(values):
    return values[:, 2:-2, 2:-2]


def taylor(wide_state, wide_sound, depth, cells, row_count):
    keep = inside_rows(0, wide_state.shape[3], depth, row_count)
    series = jnp.where(keep, wide_state, 0.0)
    running = wide_state[:, :, depth:depth + cells, depth:depth + row_count]
    for degree in range(1, ORDER + 1):
        edge = 2 * (degree - 1)
        sound = wide_sound[:, edge:wide_sound.shape[1] - edge, edge:wide_sound.shape[2] - edge]
        series = TIME_STEP / degree * operator_core(
            sound * series[0], series[1], series[2], series[3]
        )
        margin = depth - 2 * degree
        keep = inside_rows(2 * degree, series.shape[3], depth, row_count)
        series = jnp.where(keep, series, 0.0)
        running = running + series[:, :, margin:margin + cells, margin:margin + row_count]
    return running


def remap(state, offsets):
    fields, depth, cells, rows = state.shape
    planes = state.reshape(fields * depth, cells, rows)
    whole = lax.all_to_all(planes, "azi", 0, 1, tiled=True)
    total = whole.shape[1]
    for bit_pos in range((total - 1).bit_length()):
        chosen = (offsets >> bit_pos) & 1 == 1
        whole = jnp.where(chosen[None, None, :], jnp.roll(whole, 1 << bit_pos, axis=1), whole)
    planes = lax.all_to_all(whole, "azi", 1, 0, tiled=True)
    return planes.reshape(fields, depth, cells, rows)


def per_device(gas_state, sound_sq, offsets):
    depth = 2 * ORDER
    cells, row_count = gas_state.shape[2], gas_state.shape[3]

    def one_step(timestep, state):
        wide = extended(jnp.concatenate([state, sound_sq[None]]), depth)
        running = taylor(wide[:4], wide[4], depth, cells, row_count)
        return remap(running, offsets)

    return lax.fori_loop(0, STEPS, one_step, gas_state)


def solution(mesh):
    in_specs = (P(None, None, "azi", "rad"), P(None, "azi", "rad"), P("rad"))
    out_specs = P(None, None, "azi", "rad")
    return jax.shard_map(
        per_device, mesh=mesh, in_specs=in_specs, out_specs=out_specs, check_vma=False
    )
```

```python
import jax
import jax.numpy as jnp
from jax import lax
from jax.sharding import PartitionSpec as P

ORDER = 4
STEPS = 2


TIME_STEP = 0.5
ANGULAR_RATE = 1.0
SHEAR_RATE = 1.5


def ring(axis, by):
    count = lax.axis_size(axis)
    return [(i, (i + by) % count) for i in range(count)]


def window(values, start, length, which_dim):
    return lax.slice_in_dim(values, start, start + length, axis=which_dim)


def diff_along(values, which_dim):
    length = values.shape[which_dim] - 4
    return (
        8.0 * (window(values, 3, length, which_dim) - window(values, 1, length, which_dim))
        - (window(values, 4, length, which_dim) - window(values, 0, length, which_dim))
    ) / 12.0


def diff_vertical(values):
    return (
        8.0 * (jnp.roll(values, -1, 0) - jnp.roll(values, 1, 0))
        - (jnp.roll(values, -2, 0) - jnp.roll(values, 2, 0))
    ) / 12.0


def extended(cells, depth):
    count = cells.shape[2]
    cells = jnp.concatenate(
        [
            lax.ppermute(cells[:, :, count - depth:, :], "azi", ring("azi", 1)),
            cells,
            lax.ppermute(cells[:, :, :depth, :], "azi", ring("azi", -1)),
        ],
        axis=2,
    )
    rows = cells.shape[3]
    low = jnp.swapaxes(cells[..., rows - depth:], 2, 3)
    high = jnp.swapaxes(cells[..., :depth], 2, 3)
    low = jnp.swapaxes(lax.ppermute(low, "rad", ring("rad", 1)), 2, 3)
    high = jnp.swapaxes(lax.ppermute(high, "rad", ring("rad", -1)), 2, 3)
    return jnp.concatenate([low, cells, high], axis=3)


def inside_rows(start, extent, depth, row_count):
    global_row = (
        lax.axis_index("rad") * row_count - depth + start + jnp.arange(extent, dtype=jnp.int32)
    )
    return (global_row >= 0) & (global_row < row_count * lax.axis_size("rad"))


def operator_core(pressure, radial_flow, azimuth_flow, vertical_flow):
    density_rate = -(
        diff_along(radial_flow[:, 2:-2, :], 2)
        + diff_along(azimuth_flow[:, :, 2:-2], 1)
        + diff_vertical(inner_part(vertical_flow))
    )
    radial_rate = -diff_along(pressure[:, 2:-2, :], 2) + 2.0 * ANGULAR_RATE * inner_part(
        azimuth_flow
    )
    azimuth_rate = -diff_along(pressure[:, :, 2:-2], 1) - (
        2.0 - SHEAR_RATE
    ) * ANGULAR_RATE * inner_part(radial_flow)
    vertical_rate = -diff_vertical(inner_part(pressure))
    return jnp.stack([density_rate, radial_rate, azimuth_rate, vertical_rate])


def inner_part(values):
    return values[:, 2:-2, 2:-2]


def taylor(wide_state, wide_sound, depth, cells, row_count):
    keep = inside_rows(0, wide_state.shape[3], depth, row_count)
    series = jnp.where(keep, wide_state, 0.0)
    running = wide_state[:, :, depth:depth + cells, depth:depth + row_count]
    for degree in range(1, ORDER + 1):
        edge = 2 * (degree - 1)
        sound = wide_sound[:, edge:wide_sound.shape[1] - edge, edge:wide_sound.shape[2] - edge]
        series = TIME_STEP / degree * operator_core(
            sound * series[0], series[1], series[2], series[3]
        )
        margin = depth - 2 * degree
        keep = inside_rows(2 * degree, series.shape[3], depth, row_count)
        series = jnp.where(keep, series, 0.0)
        running = running + series[:, :, margin:margin + cells, margin:margin + row_count]
    return running


def roll_cells(blocks, shift):
    cells = blocks.shape[2]
    whole, part = divmod(shift, cells)
    if whole:
        blocks = jnp.roll(blocks, whole, axis=0)
    if part:
        carried = jnp.roll(blocks, 1, axis=0)
        blocks = jnp.concatenate(
            [carried[:, :, cells - part:], blocks[:, :, :cells - part]], axis=2
        )
    return blocks


def remap(state, offsets):
    fields, levels, cells, rows = state.shape
    peers = lax.axis_size("azi")
    planes = state.reshape(peers, fields * levels // peers, cells, rows)
    blocks = lax.all_to_all(planes, "azi", 0, 0, tiled=True)
    total = peers * cells
    for bit_pos in range((total - 1).bit_length()):
        chosen = (offsets >> bit_pos) & 1 == 1
        blocks = jnp.where(chosen, roll_cells(blocks, 1 << bit_pos), blocks)
    planes = lax.all_to_all(blocks, "azi", 0, 0, tiled=True)
    return planes.reshape(fields, levels, cells, rows)


def per_device(gas_state, sound_sq, offsets):
    depth = 2 * ORDER
    cells, row_count = gas_state.shape[2], gas_state.shape[3]
    wide = extended(jnp.concatenate([gas_state, sound_sq[None]]), depth)
    wide_state, wide_sound = wide[:4], wide[4]
    for timestep in range(STEPS):
        if timestep:
            wide_state = extended(state, depth)
        running = taylor(wide_state, wide_sound, depth, cells, row_count)
        state = remap(running, offsets)
    return state


def solution(mesh):
    in_specs = (P(None, None, "azi", "rad"), P(None, "azi", "rad"), P("rad"))
    out_specs = P(None, None, "azi", "rad")
    return jax.shard_map(
        per_device, mesh=mesh, in_specs=in_specs, out_specs=out_specs, check_vma=False
    )
```

```python
import jax
import jax.numpy as jnp
from jax import lax
from jax.sharding import PartitionSpec as P
from jax.experimental import pallas as pl
from jax.experimental.pallas import tpu as pltpu

ORDER = 4
STEPS = 2


TIME_STEP = 0.5
ANGULAR_RATE = 1.0
SHEAR_RATE = 1.5


def ring(axis, by):
    count = lax.axis_size(axis)
    return [(i, (i + by) % count) for i in range(count)]


def window(values, start, length, which_dim):
    return lax.slice_in_dim(values, start, start + length, axis=which_dim)


def diff_along(values, which_dim):
    length = values.shape[which_dim] - 4
    return (
        8.0 * (window(values, 3, length, which_dim) - window(values, 1, length, which_dim))
        - (window(values, 4, length, which_dim) - window(values, 0, length, which_dim))
    ) / 12.0


def diff_vertical(values):
    return (
        8.0 * (jnp.roll(values, -1, 0) - jnp.roll(values, 1, 0))
        - (jnp.roll(values, -2, 0) - jnp.roll(values, 2, 0))
    ) / 12.0


def extended(cells, depth):
    count = cells.shape[2]
    cells = jnp.concatenate(
        [
            lax.ppermute(cells[:, :, count - depth:, :], "azi", ring("azi", 1)),
            cells,
            lax.ppermute(cells[:, :, :depth, :], "azi", ring("azi", -1)),
        ],
        axis=2,
    )
    rows = cells.shape[3]
    low = jnp.swapaxes(cells[..., rows - depth:], 2, 3)
    high = jnp.swapaxes(cells[..., :depth], 2, 3)
    low = jnp.swapaxes(lax.ppermute(low, "rad", ring("rad", 1)), 2, 3)
    high = jnp.swapaxes(lax.ppermute(high, "rad", ring("rad", -1)), 2, 3)
    return jnp.concatenate([low, cells, high], axis=3)


def inside_rows(start, extent, depth, row_count):
    global_row = (
        lax.axis_index("rad") * row_count - depth + start + jnp.arange(extent, dtype=jnp.int32)
    )
    return (global_row >= 0) & (global_row < row_count * lax.axis_size("rad"))


def operator_core(pressure, radial_flow, azimuth_flow, vertical_flow):
    density_rate = -(
        diff_along(radial_flow[:, 2:-2, :], 2)
        + diff_along(azimuth_flow[:, :, 2:-2], 1)
        + diff_vertical(inner_part(vertical_flow))
    )
    radial_rate = -diff_along(pressure[:, 2:-2, :], 2) + 2.0 * ANGULAR_RATE * inner_part(
        azimuth_flow
    )
    azimuth_rate = -diff_along(pressure[:, :, 2:-2], 1) - (
        2.0 - SHEAR_RATE
    ) * ANGULAR_RATE * inner_part(radial_flow)
    vertical_rate = -diff_vertical(inner_part(pressure))
    return jnp.stack([density_rate, radial_rate, azimuth_rate, vertical_rate])


def inner_part(values):
    return values[:, 2:-2, 2:-2]


def lane_diff(values):
    size = values.shape[1]
    return (
        8.0 * (pltpu.roll(values, size - 1, 1) - pltpu.roll(values, 1, 1))
        - (pltpu.roll(values, size - 2, 1) - pltpu.roll(values, 2, 1))
    ) / 12.0


def sublane_diff(values):
    size = values.shape[0]
    return (
        8.0 * (pltpu.roll(values, size - 1, 0) - pltpu.roll(values, 1, 0))
        - (pltpu.roll(values, size - 2, 0) - pltpu.roll(values, 2, 0))
    ) / 12.0


def taylor_kernel(keep_ref, sound_ref, state_ref, running_ref, even_ref, odd_ref):
    keep = keep_ref[...] != 0.0
    levels = state_ref.shape[1]

    def start(level, carry):
        for field in range(4):
            values = state_ref[field, level]
            running_ref[field, level] = values
            even_ref[field, level] = jnp.where(keep, values, 0.0)
        return carry

    lax.fori_loop(0, levels, start, 0)
    for degree in range(1, ORDER + 1):
        source, target = (even_ref, odd_ref) if degree % 2 else (odd_ref, even_ref)

        def order(level, carry, source=source, target=target, scale=TIME_STEP / degree):
            near = [lax.rem(level + step + levels, levels) for step in (1, -1, 2, -2)]

            def vertical(value_at):
                up1, down1, up2, down2 = (value_at(at) for at in near)
                return (8.0 * (up1 - down1) - (up2 - down2)) / 12.0

            radial_flow = source[1, level]
            azimuth_flow = source[2, level]
            pressure = sound_ref[level] * source[0, level]
            density_rate = -(
                lane_diff(radial_flow)
                + sublane_diff(azimuth_flow)
                + vertical(lambda at: source[3, at])
            )
            radial_rate = -lane_diff(pressure) + 2.0 * ANGULAR_RATE * azimuth_flow
            azimuth_rate = -sublane_diff(pressure) - (2.0 - SHEAR_RATE) * ANGULAR_RATE * radial_flow
            vertical_rate = -vertical(lambda at: sound_ref[at] * source[0, at])
            rates = (density_rate, radial_rate, azimuth_rate, vertical_rate)
            for field, rate in enumerate(rates):
                series = jnp.where(keep, scale * rate, 0.0)
                target[field, level] = series
                running_ref[field, level] = running_ref[field, level] + series
            return carry

        lax.fori_loop(0, levels, order, 0)


def taylor(wide_state, wide_sound, depth, cells, row_count):
    lanes = 128 * -(-wide_state.shape[3] // 128)
    extra = lanes - wide_state.shape[3]
    wide_state = jnp.pad(wide_state, ((0, 0), (0, 0), (0, 0), (0, extra)))
    wide_sound = jnp.pad(wide_sound, ((0, 0), (0, 0), (0, extra)))
    keep = inside_rows(0, lanes, depth, row_count).astype(jnp.float32)[None, :]
    whole = pl.BlockSpec(memory_space=pltpu.VMEM)
    size = wide_state.size
    running = pl.pallas_call(
        taylor_kernel,
        out_shape=jax.ShapeDtypeStruct(wide_state.shape, jnp.float32),
        in_specs=[whole, whole, whole],
        out_specs=whole,
        scratch_shapes=[pltpu.VMEM(wide_state.shape, jnp.float32)] * 2,
        compiler_params=pltpu.CompilerParams(vmem_limit_bytes=48 * 1024 * 1024),
        cost_estimate=pl.CostEstimate(
            flops=60 * ORDER * size, transcendentals=0, bytes_accessed=4 * (2 * size + size // 4)
        ),
    )(keep, wide_sound, wide_state)
    return running[:, :, depth:depth + cells, depth:depth + row_count]


def roll_cells(blocks, shift):
    cells = blocks.shape[2]
    whole, part = divmod(shift, cells)
    if whole:
        blocks = jnp.roll(blocks, whole, axis=0)
    if part:
        carried = jnp.roll(blocks, 1, axis=0)
        blocks = jnp.concatenate(
            [carried[:, :, cells - part:], blocks[:, :, :cells - part]], axis=2
        )
    return blocks


def remap(state, offsets):
    fields, levels, cells, rows = state.shape
    peers = lax.axis_size("azi")
    planes = state.reshape(peers, fields * levels // peers, cells, rows)
    blocks = lax.all_to_all(planes, "azi", 0, 0, tiled=True)
    total = peers * cells
    for bit_pos in range((total - 1).bit_length()):
        chosen = (offsets >> bit_pos) & 1 == 1
        blocks = jnp.where(chosen, roll_cells(blocks, 1 << bit_pos), blocks)
    planes = lax.all_to_all(blocks, "azi", 0, 0, tiled=True)
    return planes.reshape(fields, levels, cells, rows)


def per_device(gas_state, sound_sq, offsets):
    depth = 2 * ORDER
    cells, row_count = gas_state.shape[2], gas_state.shape[3]
    wide = extended(jnp.concatenate([gas_state, sound_sq[None]]), depth)
    wide_state, wide_sound = wide[:4], wide[4]
    for timestep in range(STEPS):
        if timestep:
            wide_state = extended(state, depth)
        running = taylor(wide_state, wide_sound, depth, cells, row_count)
        state = remap(running, offsets)
    return state


def solution(mesh):
    in_specs = (P(None, None, "azi", "rad"), P(None, "azi", "rad"), P("rad"))
    out_specs = P(None, None, "azi", "rad")
    return jax.shard_map(
        per_device, mesh=mesh, in_specs=in_specs, out_specs=out_specs, check_vma=False
    )
```

```python
import jax
import jax.numpy as jnp
from jax import lax
from jax.sharding import PartitionSpec as P
from jax.experimental import pallas as pl
from jax.experimental.pallas import tpu as pltpu

ORDER = 4
STEPS = 2


TIME_STEP = 0.5
ANGULAR_RATE = 1.0
SHEAR_RATE = 1.5


def ring(axis, by):
    count = lax.axis_size(axis)
    return [(i, (i + by) % count) for i in range(count)]


def window(values, start, length, which_dim):
    return lax.slice_in_dim(values, start, start + length, axis=which_dim)


def diff_along(values, which_dim):
    length = values.shape[which_dim] - 4
    return (
        8.0 * (window(values, 3, length, which_dim) - window(values, 1, length, which_dim))
        - (window(values, 4, length, which_dim) - window(values, 0, length, which_dim))
    ) / 12.0


def diff_vertical(values):
    return (
        8.0 * (jnp.roll(values, -1, 0) - jnp.roll(values, 1, 0))
        - (jnp.roll(values, -2, 0) - jnp.roll(values, 2, 0))
    ) / 12.0


def azimuthal_halos(cells, depth):
    count = cells.shape[2]
    return jnp.concatenate(
        [
            lax.ppermute(cells[:, :, count - depth:, :], "azi", ring("azi", 1)),
            cells,
            lax.ppermute(cells[:, :, :depth, :], "azi", ring("azi", -1)),
        ],
        axis=2,
    )


def radial_halos(cells, depth):
    rows = cells.shape[3]
    low = jnp.swapaxes(cells[..., rows - depth:], 2, 3)
    high = jnp.swapaxes(cells[..., :depth], 2, 3)
    low = jnp.swapaxes(lax.ppermute(low, "rad", ring("rad", 1)), 2, 3)
    high = jnp.swapaxes(lax.ppermute(high, "rad", ring("rad", -1)), 2, 3)
    return jnp.concatenate([low, cells, high], axis=3)


def extended(cells, depth):
    return radial_halos(azimuthal_halos(cells, depth), depth)


def inside_rows(start, extent, depth, row_count):
    global_row = (
        lax.axis_index("rad") * row_count - depth + start + jnp.arange(extent, dtype=jnp.int32)
    )
    return (global_row >= 0) & (global_row < row_count * lax.axis_size("rad"))


def operator_core(pressure, radial_flow, azimuth_flow, vertical_flow):
    density_rate = -(
        diff_along(radial_flow[:, 2:-2, :], 2)
        + diff_along(azimuth_flow[:, :, 2:-2], 1)
        + diff_vertical(inner_part(vertical_flow))
    )
    radial_rate = -diff_along(pressure[:, 2:-2, :], 2) + 2.0 * ANGULAR_RATE * inner_part(
        azimuth_flow
    )
    azimuth_rate = -diff_along(pressure[:, :, 2:-2], 1) - (
        2.0 - SHEAR_RATE
    ) * ANGULAR_RATE * inner_part(radial_flow)
    vertical_rate = -diff_vertical(inner_part(pressure))
    return jnp.stack([density_rate, radial_rate, azimuth_rate, vertical_rate])


def inner_part(values):
    return values[:, 2:-2, 2:-2]


def lane_diff(values):
    size = values.shape[1]
    return (
        8.0 * (pltpu.roll(values, size - 1, 1) - pltpu.roll(values, 1, 1))
        - (pltpu.roll(values, size - 2, 1) - pltpu.roll(values, 2, 1))
    ) / 12.0


def sublane_diff(values):
    size = values.shape[0]
    return (
        8.0 * (pltpu.roll(values, size - 1, 0) - pltpu.roll(values, 1, 0))
        - (pltpu.roll(values, size - 2, 0) - pltpu.roll(values, 2, 0))
    ) / 12.0


def taylor_kernel(keep_ref, sound_ref, state_ref, running_ref, even_ref, odd_ref):
    keep = keep_ref[...] != 0.0
    levels = state_ref.shape[1]

    def start(level, carry):
        for field in range(4):
            values = state_ref[field, level]
            running_ref[field, level] = values
            even_ref[field, level] = jnp.where(keep, values, 0.0)
        return carry

    lax.fori_loop(0, levels, start, 0)
    for degree in range(1, ORDER + 1):
        source, target = (even_ref, odd_ref) if degree % 2 else (odd_ref, even_ref)

        def order(level, carry, source=source, target=target, scale=TIME_STEP / degree):
            near = [lax.rem(level + step + levels, levels) for step in (1, -1, 2, -2)]

            def vertical(value_at):
                up1, down1, up2, down2 = (value_at(at) for at in near)
                return (8.0 * (up1 - down1) - (up2 - down2)) / 12.0

            radial_flow = source[1, level]
            azimuth_flow = source[2, level]
            pressure = sound_ref[level] * source[0, level]
            density_rate = -(
                lane_diff(radial_flow)
                + sublane_diff(azimuth_flow)
                + vertical(lambda at: source[3, at])
            )
            radial_rate = -lane_diff(pressure) + 2.0 * ANGULAR_RATE * azimuth_flow
            azimuth_rate = -sublane_diff(pressure) - (2.0 - SHEAR_RATE) * ANGULAR_RATE * radial_flow
            vertical_rate = -vertical(lambda at: sound_ref[at] * source[0, at])
            rates = (density_rate, radial_rate, azimuth_rate, vertical_rate)
            for field, rate in enumerate(rates):
                series = jnp.where(keep, scale * rate, 0.0)
                target[field, level] = series
                running_ref[field, level] = running_ref[field, level] + series
            return carry

        lax.fori_loop(0, levels, order, 0)


def taylor(wide_state, wide_sound, depth, cells, row_count):
    lanes = 128 * -(-wide_state.shape[3] // 128)
    extra = lanes - wide_state.shape[3]
    wide_state = jnp.pad(wide_state, ((0, 0), (0, 0), (0, 0), (0, extra)))
    wide_sound = jnp.pad(wide_sound, ((0, 0), (0, 0), (0, extra)))
    keep = inside_rows(0, lanes, depth, row_count).astype(jnp.float32)[None, :]
    whole = pl.BlockSpec(memory_space=pltpu.VMEM)
    size = wide_state.size
    running = pl.pallas_call(
        taylor_kernel,
        out_shape=jax.ShapeDtypeStruct(wide_state.shape, jnp.float32),
        in_specs=[whole, whole, whole],
        out_specs=whole,
        scratch_shapes=[pltpu.VMEM(wide_state.shape, jnp.float32)] * 2,
        compiler_params=pltpu.CompilerParams(vmem_limit_bytes=48 * 1024 * 1024),
        cost_estimate=pl.CostEstimate(
            flops=60 * ORDER * size, transcendentals=0, bytes_accessed=4 * (2 * size + size // 4)
        ),
    )(keep, wide_sound, wide_state)
    return running[:, :, depth:depth + cells, depth:depth + row_count]


def roll_cells(blocks, shift):
    cells = blocks.shape[2]
    whole, part = divmod(shift, cells)
    if whole:
        blocks = jnp.roll(blocks, whole, axis=0)
    if part:
        carried = jnp.roll(blocks, 1, axis=0)
        blocks = jnp.concatenate(
            [carried[:, :, cells - part:], blocks[:, :, :cells - part]], axis=2
        )
    return blocks


def remap(state, offsets, depth):
    fields, levels, cells, rows = state.shape
    peers = lax.axis_size("azi")
    planes = state.reshape(peers, fields * levels // peers, cells, rows)
    blocks = lax.all_to_all(planes, "azi", 0, 0, tiled=True)
    total = peers * cells
    for bit_pos in range((total - 1).bit_length()):
        chosen = (offsets >> bit_pos) & 1 == 1
        blocks = jnp.where(chosen, roll_cells(blocks, 1 << bit_pos), blocks)
    if depth:
        blocks = jnp.concatenate(
            [jnp.roll(blocks, 1, axis=0)[:, :, cells - depth:], blocks,
             jnp.roll(blocks, -1, axis=0)[:, :, :depth]],
            axis=2,
        )
    planes = lax.all_to_all(blocks, "azi", 0, 0, tiled=True)
    return planes.reshape(fields, levels, cells + 2 * depth, rows)


def per_device(gas_state, sound_sq, offsets):
    depth = 2 * ORDER
    cells, row_count = gas_state.shape[2], gas_state.shape[3]
    wide = extended(jnp.concatenate([gas_state, sound_sq[None]]), depth)
    wide_state, wide_sound = wide[:4], wide[4]
    for timestep in range(STEPS):
        running = taylor(wide_state, wide_sound, depth, cells, row_count)
        last = timestep == STEPS - 1
        state = remap(running, offsets, 0 if last else depth)
        if not last:
            wide_state = radial_halos(state, depth)
    return state


def solution(mesh):
    in_specs = (P(None, None, "azi", "rad"), P(None, "azi", "rad"), P("rad"))
    out_specs = P(None, None, "azi", "rad")
    return jax.shard_map(
        per_device, mesh=mesh, in_specs=in_specs, out_specs=out_specs, check_vma=False
    )
```

```python
import jax
import jax.numpy as jnp
from jax import lax
from jax.sharding import PartitionSpec as P
from jax.experimental import pallas as pl
from jax.experimental.pallas import tpu as pltpu

ORDER = 4
STEPS = 2


TIME_STEP = 0.5
ANGULAR_RATE = 1.0
SHEAR_RATE = 1.5


def ring(axis, by):
    count = lax.axis_size(axis)
    return [(i, (i + by) % count) for i in range(count)]


def window(values, start, length, which_dim):
    return lax.slice_in_dim(values, start, start + length, axis=which_dim)


def diff_along(values, which_dim):
    length = values.shape[which_dim] - 4
    return (
        8.0 * (window(values, 3, length, which_dim) - window(values, 1, length, which_dim))
        - (window(values, 4, length, which_dim) - window(values, 0, length, which_dim))
    ) / 12.0


def diff_vertical(values):
    return (
        8.0 * (jnp.roll(values, -1, 0) - jnp.roll(values, 1, 0))
        - (jnp.roll(values, -2, 0) - jnp.roll(values, 2, 0))
    ) / 12.0


def azimuthal_halos(cells, depth):
    count = cells.shape[2]
    return jnp.concatenate(
        [
            lax.ppermute(cells[:, :, count - depth:, :], "azi", ring("azi", 1)),
            cells,
            lax.ppermute(cells[:, :, :depth, :], "azi", ring("azi", -1)),
        ],
        axis=2,
    )


def radial_halos(cells, depth):
    rows = cells.shape[3]
    low = jnp.swapaxes(cells[..., rows - depth:], 2, 3)
    high = jnp.swapaxes(cells[..., :depth], 2, 3)
    low = jnp.swapaxes(lax.ppermute(low, "rad", ring("rad", 1)), 2, 3)
    high = jnp.swapaxes(lax.ppermute(high, "rad", ring("rad", -1)), 2, 3)
    lanes = 128 * -(-(rows + 2 * depth) // 128)
    unused = jnp.zeros(cells.shape[:3] + (lanes - rows - 2 * depth,), cells.dtype)
    return jnp.concatenate([cells, high, unused, low], axis=3)


def extended(cells, depth):
    return radial_halos(azimuthal_halos(cells, depth), depth)


def inside_rows(lanes, depth, row_count):
    lane = jnp.arange(lanes, dtype=jnp.int32)
    lane = jnp.where(lane >= lanes - depth, lane - lanes, lane)
    global_row = lax.axis_index("rad") * row_count + lane
    return (global_row >= 0) & (global_row < row_count * lax.axis_size("rad"))


def operator_core(pressure, radial_flow, azimuth_flow, vertical_flow):
    density_rate = -(
        diff_along(radial_flow[:, 2:-2, :], 2)
        + diff_along(azimuth_flow[:, :, 2:-2], 1)
        + diff_vertical(inner_part(vertical_flow))
    )
    radial_rate = -diff_along(pressure[:, 2:-2, :], 2) + 2.0 * ANGULAR_RATE * inner_part(
        azimuth_flow
    )
    azimuth_rate = -diff_along(pressure[:, :, 2:-2], 1) - (
        2.0 - SHEAR_RATE
    ) * ANGULAR_RATE * inner_part(radial_flow)
    vertical_rate = -diff_vertical(inner_part(pressure))
    return jnp.stack([density_rate, radial_rate, azimuth_rate, vertical_rate])


def inner_part(values):
    return values[:, 2:-2, 2:-2]


def lane_diff(values):
    size = values.shape[1]
    return (
        8.0 * (pltpu.roll(values, size - 1, 1) - pltpu.roll(values, 1, 1))
        - (pltpu.roll(values, size - 2, 1) - pltpu.roll(values, 2, 1))
    ) / 12.0


def sublane_diff(values):
    size = values.shape[0]
    return (
        8.0 * (pltpu.roll(values, size - 1, 0) - pltpu.roll(values, 1, 0))
        - (pltpu.roll(values, size - 2, 0) - pltpu.roll(values, 2, 0))
    ) / 12.0


def taylor_kernel(keep_ref, sound_ref, state_ref, running_ref, even_ref, odd_ref):
    keep = keep_ref[...] != 0.0
    levels = state_ref.shape[1]

    def start(level, carry):
        for field in range(4):
            values = state_ref[field, level]
            running_ref[field, level] = values
            even_ref[field, level] = jnp.where(keep, values, 0.0)
        return carry

    lax.fori_loop(0, levels, start, 0)
    for degree in range(1, ORDER + 1):
        source, target = (even_ref, odd_ref) if degree % 2 else (odd_ref, even_ref)

        def order(level, carry, source=source, target=target, scale=TIME_STEP / degree):
            near = [lax.rem(level + step + levels, levels) for step in (1, -1, 2, -2)]

            def vertical(value_at):
                up1, down1, up2, down2 = (value_at(at) for at in near)
                return (8.0 * (up1 - down1) - (up2 - down2)) / 12.0

            radial_flow = source[1, level]
            azimuth_flow = source[2, level]
            pressure = sound_ref[level] * source[0, level]
            density_rate = -(
                lane_diff(radial_flow)
                + sublane_diff(azimuth_flow)
                + vertical(lambda at: source[3, at])
            )
            radial_rate = -lane_diff(pressure) + 2.0 * ANGULAR_RATE * azimuth_flow
            azimuth_rate = -sublane_diff(pressure) - (2.0 - SHEAR_RATE) * ANGULAR_RATE * radial_flow
            vertical_rate = -vertical(lambda at: sound_ref[at] * source[0, at])
            rates = (density_rate, radial_rate, azimuth_rate, vertical_rate)
            for field, rate in enumerate(rates):
                series = jnp.where(keep, scale * rate, 0.0)
                target[field, level] = series
                running_ref[field, level] = running_ref[field, level] + series
            return carry

        lax.fori_loop(0, levels, order, 0)


def taylor(wide_state, wide_sound, depth, cells, row_count):
    keep = inside_rows(wide_state.shape[3], depth, row_count).astype(jnp.float32)[None, :]
    whole = pl.BlockSpec(memory_space=pltpu.VMEM)
    size = wide_state.size
    running = pl.pallas_call(
        taylor_kernel,
        out_shape=jax.ShapeDtypeStruct(wide_state.shape, jnp.float32),
        in_specs=[whole, whole, whole],
        out_specs=whole,
        scratch_shapes=[pltpu.VMEM(wide_state.shape, jnp.float32)] * 2,
        compiler_params=pltpu.CompilerParams(vmem_limit_bytes=48 * 1024 * 1024),
        cost_estimate=pl.CostEstimate(
            flops=60 * ORDER * size, transcendentals=0, bytes_accessed=4 * (2 * size + size // 4)
        ),
    )(keep, wide_sound, wide_state)
    return running[:, :, depth:depth + cells, :row_count]


def roll_cells(blocks, shift):
    cells = blocks.shape[2]
    whole, part = divmod(shift, cells)
    if whole:
        blocks = jnp.roll(blocks, whole, axis=0)
    if part:
        carried = jnp.roll(blocks, 1, axis=0)
        blocks = jnp.concatenate(
            [carried[:, :, cells - part:], blocks[:, :, :cells - part]], axis=2
        )
    return blocks


def remap(state, offsets, depth):
    fields, levels, cells, rows = state.shape
    peers = lax.axis_size("azi")
    planes = state.reshape(peers, fields * levels // peers, cells, rows)
    blocks = lax.all_to_all(planes, "azi", 0, 0, tiled=True)
    total = peers * cells
    for bit_pos in range((total - 1).bit_length()):
        chosen = (offsets >> bit_pos) & 1 == 1
        blocks = jnp.where(chosen, roll_cells(blocks, 1 << bit_pos), blocks)
    if depth:
        blocks = jnp.concatenate(
            [jnp.roll(blocks, 1, axis=0)[:, :, cells - depth:], blocks,
             jnp.roll(blocks, -1, axis=0)[:, :, :depth]],
            axis=2,
        )
    planes = lax.all_to_all(blocks, "azi", 0, 0, tiled=True)
    return planes.reshape(fields, levels, cells + 2 * depth, rows)


def per_device(gas_state, sound_sq, offsets):
    depth = 2 * ORDER
    cells, row_count = gas_state.shape[2], gas_state.shape[3]
    wide = extended(jnp.concatenate([gas_state, sound_sq[None]]), depth)
    wide_state, wide_sound = wide[:4], wide[4]
    for timestep in range(STEPS):
        running = taylor(wide_state, wide_sound, depth, cells, row_count)
        last = timestep == STEPS - 1
        state = remap(running, offsets, 0 if last else depth)
        if not last:
            wide_state = radial_halos(state, depth)
    return state


def solution(mesh):
    in_specs = (P(None, None, "azi", "rad"), P(None, "azi", "rad"), P("rad"))
    out_specs = P(None, None, "azi", "rad")
    return jax.shard_map(
        per_device, mesh=mesh, in_specs=in_specs, out_specs=out_specs, check_vma=False
    )
```

```python
import functools

import jax
import jax.numpy as jnp
from jax import lax
from jax.sharding import PartitionSpec as P
from jax.experimental import pallas as pl
from jax.experimental.pallas import tpu as pltpu

ORDER = 4
STEPS = 2


TIME_STEP = 0.5
ANGULAR_RATE = 1.0
SHEAR_RATE = 1.5


def ring(axis, by):
    count = lax.axis_size(axis)
    return [(i, (i + by) % count) for i in range(count)]


def window(values, start, length, which_dim):
    return lax.slice_in_dim(values, start, start + length, axis=which_dim)


def diff_along(values, which_dim):
    length = values.shape[which_dim] - 4
    return (
        8.0 * (window(values, 3, length, which_dim) - window(values, 1, length, which_dim))
        - (window(values, 4, length, which_dim) - window(values, 0, length, which_dim))
    ) / 12.0


def diff_vertical(values):
    return (
        8.0 * (jnp.roll(values, -1, 0) - jnp.roll(values, 1, 0))
        - (jnp.roll(values, -2, 0) - jnp.roll(values, 2, 0))
    ) / 12.0


def azimuthal_halos(cells, depth):
    count = cells.shape[2]
    return jnp.concatenate(
        [
            lax.ppermute(cells[:, :, count - depth:, :], "azi", ring("azi", 1)),
            cells,
            lax.ppermute(cells[:, :, :depth, :], "azi", ring("azi", -1)),
        ],
        axis=2,
    )


def radial_halos(cells, depth):
    rows = cells.shape[3]
    low = jnp.swapaxes(cells[..., rows - depth:], 2, 3)
    high = jnp.swapaxes(cells[..., :depth], 2, 3)
    low = jnp.swapaxes(lax.ppermute(low, "rad", ring("rad", 1)), 2, 3)
    high = jnp.swapaxes(lax.ppermute(high, "rad", ring("rad", -1)), 2, 3)
    lanes = 128 * -(-(rows + 2 * depth) // 128)
    unused = jnp.zeros(cells.shape[:3] + (lanes - rows - 2 * depth,), cells.dtype)
    return jnp.concatenate([cells, high, unused, low], axis=3)


def extended(cells, depth):
    return radial_halos(azimuthal_halos(cells, depth), depth)


def inside_rows(lanes, depth, row_count):
    lane = jnp.arange(lanes, dtype=jnp.int32)
    lane = jnp.where(lane >= lanes - depth, lane - lanes, lane)
    global_row = lax.axis_index("rad") * row_count + lane
    return (global_row >= 0) & (global_row < row_count * lax.axis_size("rad"))


def operator_core(pressure, radial_flow, azimuth_flow, vertical_flow):
    density_rate = -(
        diff_along(radial_flow[:, 2:-2, :], 2)
        + diff_along(azimuth_flow[:, :, 2:-2], 1)
        + diff_vertical(inner_part(vertical_flow))
    )
    radial_rate = -diff_along(pressure[:, 2:-2, :], 2) + 2.0 * ANGULAR_RATE * inner_part(
        azimuth_flow
    )
    azimuth_rate = -diff_along(pressure[:, :, 2:-2], 1) - (
        2.0 - SHEAR_RATE
    ) * ANGULAR_RATE * inner_part(radial_flow)
    vertical_rate = -diff_vertical(inner_part(pressure))
    return jnp.stack([density_rate, radial_rate, azimuth_rate, vertical_rate])


def inner_part(values):
    return values[:, 2:-2, 2:-2]


def lane_diff(values):
    size = values.shape[1]
    return (
        8.0 * (pltpu.roll(values, size - 1, 1) - pltpu.roll(values, 1, 1))
        - (pltpu.roll(values, size - 2, 1) - pltpu.roll(values, 2, 1))
    ) / 12.0


def sublane_diff(values):
    size = values.shape[0]
    return (
        8.0 * (pltpu.roll(values, size - 1, 0) - pltpu.roll(values, 1, 0))
        - (pltpu.roll(values, size - 2, 0) - pltpu.roll(values, 2, 0))
    ) / 12.0


def taylor_kernel(keep_ref, sound_ref, state_ref, running_ref, even_ref, odd_ref, own):
    keep = keep_ref[...] != 0.0
    levels = state_ref.shape[1]
    first, cells, rows = own

    def start(level, carry):
        for field in range(4):
            values = state_ref[field, level]
            running_ref[field, level] = values
            even_ref[field, level] = jnp.where(keep, values, 0.0)
        return carry

    lax.fori_loop(0, levels, start, 0)
    for degree in range(1, ORDER + 1):
        source, target = (even_ref, odd_ref) if degree % 2 else (odd_ref, even_ref)
        last = degree == ORDER
        region = (slice(first, first + cells), slice(0, rows)) if last else (slice(None), slice(None))

        def order(level, carry, source=source, target=target, scale=TIME_STEP / degree,
                  last=last, region=region):
            near = [lax.rem(level + step + levels, levels) for step in (1, -1, 2, -2)]

            def vertical(value_at):
                up1, down1, up2, down2 = (value_at(at) for at in near)
                return (8.0 * (up1 - down1) - (up2 - down2)) / 12.0

            radial_flow = source[1, level]
            azimuth_flow = source[2, level]
            pressure = sound_ref[level] * source[0, level]
            density_rate = -(
                lane_diff(radial_flow)[region]
                + sublane_diff(azimuth_flow)[region]
                + vertical(lambda at: source[3, at][region])
            )
            radial_rate = -lane_diff(pressure)[region] + 2.0 * ANGULAR_RATE * azimuth_flow[region]
            azimuth_rate = -sublane_diff(pressure)[region] - (
                2.0 - SHEAR_RATE
            ) * ANGULAR_RATE * radial_flow[region]
            vertical_rate = -vertical(lambda at: sound_ref[at][region] * source[0, at][region])
            rates = (density_rate, radial_rate, azimuth_rate, vertical_rate)
            inside = keep[:, region[1]]
            for field, rate in enumerate(rates):
                series = jnp.where(inside, scale * rate, 0.0)
                if not last:
                    target[field, level] = series
                running_ref[field, level, region[0], region[1]] = (
                    running_ref[field, level, region[0], region[1]] + series
                )
            return carry

        lax.fori_loop(0, levels, order, 0)


def taylor(wide_state, wide_sound, depth, cells, row_count):
    keep = inside_rows(wide_state.shape[3], depth, row_count).astype(jnp.float32)[None, :]
    whole = pl.BlockSpec(memory_space=pltpu.VMEM)
    size = wide_state.size
    running = pl.pallas_call(
        functools.partial(taylor_kernel, own=(depth, cells, row_count)),
        out_shape=jax.ShapeDtypeStruct(wide_state.shape, jnp.float32),
        in_specs=[whole, whole, whole],
        out_specs=whole,
        scratch_shapes=[pltpu.VMEM(wide_state.shape, jnp.float32)] * 2,
        compiler_params=pltpu.CompilerParams(vmem_limit_bytes=48 * 1024 * 1024),
        cost_estimate=pl.CostEstimate(
            flops=60 * ORDER * size, transcendentals=0, bytes_accessed=4 * (2 * size + size // 4)
        ),
    )(keep, wide_sound, wide_state)
    return running[:, :, depth:depth + cells, :row_count]


def roll_cells(blocks, shift):
    cells = blocks.shape[2]
    whole, part = divmod(shift, cells)
    if whole:
        blocks = jnp.roll(blocks, whole, axis=0)
    if part:
        carried = jnp.roll(blocks, 1, axis=0)
        blocks = jnp.concatenate(
            [carried[:, :, cells - part:], blocks[:, :, :cells - part]], axis=2
        )
    return blocks


def remap(state, offsets, depth):
    fields, levels, cells, rows = state.shape
    peers = lax.axis_size("azi")
    planes = state.reshape(peers, fields * levels // peers, cells, rows)
    blocks = lax.all_to_all(planes, "azi", 0, 0, tiled=True)
    total = peers * cells
    for bit_pos in range((total - 1).bit_length()):
        chosen = (offsets >> bit_pos) & 1 == 1
        blocks = jnp.where(chosen, roll_cells(blocks, 1 << bit_pos), blocks)
    if depth:
        blocks = jnp.concatenate(
            [jnp.roll(blocks, 1, axis=0)[:, :, cells - depth:], blocks,
             jnp.roll(blocks, -1, axis=0)[:, :, :depth]],
            axis=2,
        )
    planes = lax.all_to_all(blocks, "azi", 0, 0, tiled=True)
    return planes.reshape(fields, levels, cells + 2 * depth, rows)


def per_device(gas_state, sound_sq, offsets):
    depth = 2 * ORDER
    cells, row_count = gas_state.shape[2], gas_state.shape[3]
    wide = extended(jnp.concatenate([gas_state, sound_sq[None]]), depth)
    wide_state, wide_sound = wide[:4], wide[4]
    for timestep in range(STEPS):
        running = taylor(wide_state, wide_sound, depth, cells, row_count)
        last = timestep == STEPS - 1
        state = remap(running, offsets, 0 if last else depth)
        if not last:
            wide_state = radial_halos(state, depth)
    return state


def solution(mesh):
    in_specs = (P(None, None, "azi", "rad"), P(None, "azi", "rad"), P("rad"))
    out_specs = P(None, None, "azi", "rad")
    return jax.shard_map(
        per_device, mesh=mesh, in_specs=in_specs, out_specs=out_specs, check_vma=False
    )
```

```python
import functools

import jax
import jax.numpy as jnp
from jax import lax
from jax.sharding import PartitionSpec as P
from jax.experimental import pallas as pl
from jax.experimental.pallas import tpu as pltpu

ORDER = 4
STEPS = 2


TIME_STEP = 0.5
ANGULAR_RATE = 1.0
SHEAR_RATE = 1.5


def ring(axis, by):
    count = lax.axis_size(axis)
    return [(i, (i + by) % count) for i in range(count)]


def window(values, start, length, which_dim):
    return lax.slice_in_dim(values, start, start + length, axis=which_dim)


def diff_along(values, which_dim):
    length = values.shape[which_dim] - 4
    return (
        8.0 * (window(values, 3, length, which_dim) - window(values, 1, length, which_dim))
        - (window(values, 4, length, which_dim) - window(values, 0, length, which_dim))
    ) / 12.0


def diff_vertical(values):
    return (
        8.0 * (jnp.roll(values, -1, 0) - jnp.roll(values, 1, 0))
        - (jnp.roll(values, -2, 0) - jnp.roll(values, 2, 0))
    ) / 12.0


def azimuthal_halos(cells, depth):
    count = cells.shape[2]
    return jnp.concatenate(
        [
            lax.ppermute(cells[:, :, count - depth:, :], "azi", ring("azi", 1)),
            cells,
            lax.ppermute(cells[:, :, :depth, :], "azi", ring("azi", -1)),
        ],
        axis=2,
    )


def radial_halos(cells, depth):
    rows = cells.shape[3]
    low = jnp.swapaxes(cells[..., rows - depth:], 2, 3)
    high = jnp.swapaxes(cells[..., :depth], 2, 3)
    low = jnp.swapaxes(lax.ppermute(low, "rad", ring("rad", 1)), 2, 3)
    high = jnp.swapaxes(lax.ppermute(high, "rad", ring("rad", -1)), 2, 3)
    lanes = 128 * -(-(rows + 2 * depth) // 128)
    unused = jnp.zeros(cells.shape[:3] + (lanes - rows - 2 * depth,), cells.dtype)
    return jnp.concatenate([cells, high, unused, low], axis=3)


def extended(cells, depth):
    return radial_halos(azimuthal_halos(cells, depth), depth)


def inside_rows(lanes, depth, row_count):
    lane = jnp.arange(lanes, dtype=jnp.int32)
    lane = jnp.where(lane >= lanes - depth, lane - lanes, lane)
    global_row = lax.axis_index("rad") * row_count + lane
    return (global_row >= 0) & (global_row < row_count * lax.axis_size("rad"))


def operator_core(pressure, radial_flow, azimuth_flow, vertical_flow):
    density_rate = -(
        diff_along(radial_flow[:, 2:-2, :], 2)
        + diff_along(azimuth_flow[:, :, 2:-2], 1)
        + diff_vertical(inner_part(vertical_flow))
    )
    radial_rate = -diff_along(pressure[:, 2:-2, :], 2) + 2.0 * ANGULAR_RATE * inner_part(
        azimuth_flow
    )
    azimuth_rate = -diff_along(pressure[:, :, 2:-2], 1) - (
        2.0 - SHEAR_RATE
    ) * ANGULAR_RATE * inner_part(radial_flow)
    vertical_rate = -diff_vertical(inner_part(pressure))
    return jnp.stack([density_rate, radial_rate, azimuth_rate, vertical_rate])


def inner_part(values):
    return values[:, 2:-2, 2:-2]


def lane_diff(values):
    size = values.shape[1]
    return (
        8.0 * (pltpu.roll(values, size - 1, 1) - pltpu.roll(values, 1, 1))
        - (pltpu.roll(values, size - 2, 1) - pltpu.roll(values, 2, 1))
    ) / 12.0


def sublane_diff(values):
    size = values.shape[0]
    return (
        8.0 * (pltpu.roll(values, size - 1, 0) - pltpu.roll(values, 1, 0))
        - (pltpu.roll(values, size - 2, 0) - pltpu.roll(values, 2, 0))
    ) / 12.0


def taylor_kernel(keep_ref, sound_ref, state_ref, running_ref, even_ref, odd_ref, own):
    keep = keep_ref[...] != 0.0
    levels = state_ref.shape[1]
    first, cells, rows = own

    def start(level, carry):
        for field in range(4):
            values = state_ref[field, level]
            running_ref[field, level] = values[first:first + cells, :rows]
            even_ref[field, level] = jnp.where(keep, values, 0.0)
        return carry

    lax.fori_loop(0, levels, start, 0)
    for degree in range(1, ORDER + 1):
        source, target = (even_ref, odd_ref) if degree % 2 else (odd_ref, even_ref)
        last = degree == ORDER
        region = (slice(first, first + cells), slice(0, rows)) if last else (slice(None), slice(None))

        def order(level, carry, source=source, target=target, scale=TIME_STEP / degree,
                  last=last, region=region):
            near = [lax.rem(level + step + levels, levels) for step in (1, -1, 2, -2)]

            def vertical(value_at):
                up1, down1, up2, down2 = (value_at(at) for at in near)
                return (8.0 * (up1 - down1) - (up2 - down2)) / 12.0

            radial_flow = source[1, level]
            azimuth_flow = source[2, level]
            pressure = sound_ref[level] * source[0, level]
            density_rate = -(
                lane_diff(radial_flow)[region]
                + sublane_diff(azimuth_flow)[region]
                + vertical(lambda at: source[3, at][region])
            )
            radial_rate = -lane_diff(pressure)[region] + 2.0 * ANGULAR_RATE * azimuth_flow[region]
            azimuth_rate = -sublane_diff(pressure)[region] - (
                2.0 - SHEAR_RATE
            ) * ANGULAR_RATE * radial_flow[region]
            vertical_rate = -vertical(lambda at: sound_ref[at][region] * source[0, at][region])
            rates = (density_rate, radial_rate, azimuth_rate, vertical_rate)
            inside = keep[:, region[1]]
            for field, rate in enumerate(rates):
                series = jnp.where(inside, scale * rate, 0.0)
                if not last:
                    target[field, level] = series
                own_part = series if last else series[first:first + cells, :rows]
                running_ref[field, level] = running_ref[field, level] + own_part
            return carry

        lax.fori_loop(0, levels, order, 0)


def taylor(wide_state, wide_sound, depth, cells, row_count):
    keep = inside_rows(wide_state.shape[3], depth, row_count).astype(jnp.float32)[None, :]
    whole = pl.BlockSpec(memory_space=pltpu.VMEM)
    size = wide_state.size
    running = pl.pallas_call(
        functools.partial(taylor_kernel, own=(depth, cells, row_count)),
        out_shape=jax.ShapeDtypeStruct(wide_state.shape[:2] + (cells, row_count), jnp.float32),
        in_specs=[whole, whole, whole],
        out_specs=whole,
        scratch_shapes=[pltpu.VMEM(wide_state.shape, jnp.float32)] * 2,
        compiler_params=pltpu.CompilerParams(vmem_limit_bytes=48 * 1024 * 1024),
        cost_estimate=pl.CostEstimate(
            flops=60 * ORDER * size, transcendentals=0, bytes_accessed=4 * (2 * size + size // 4)
        ),
    )(keep, wide_sound, wide_state)
    return running


def roll_cells(blocks, shift):
    cells = blocks.shape[2]
    whole, part = divmod(shift, cells)
    if whole:
        blocks = jnp.roll(blocks, whole, axis=0)
    if part:
        carried = jnp.roll(blocks, 1, axis=0)
        blocks = jnp.concatenate(
            [carried[:, :, cells - part:], blocks[:, :, :cells - part]], axis=2
        )
    return blocks


def remap(state, offsets, depth):
    fields, levels, cells, rows = state.shape
    peers = lax.axis_size("azi")
    planes = state.reshape(peers, fields * levels // peers, cells, rows)
    blocks = lax.all_to_all(planes, "azi", 0, 0, tiled=True)
    total = peers * cells
    for bit_pos in range((total - 1).bit_length()):
        chosen = (offsets >> bit_pos) & 1 == 1
        blocks = jnp.where(chosen, roll_cells(blocks, 1 << bit_pos), blocks)
    if depth:
        blocks = jnp.concatenate(
            [jnp.roll(blocks, 1, axis=0)[:, :, cells - depth:], blocks,
             jnp.roll(blocks, -1, axis=0)[:, :, :depth]],
            axis=2,
        )
    planes = lax.all_to_all(blocks, "azi", 0, 0, tiled=True)
    return planes.reshape(fields, levels, cells + 2 * depth, rows)


def per_device(gas_state, sound_sq, offsets):
    depth = 2 * ORDER
    cells, row_count = gas_state.shape[2], gas_state.shape[3]
    wide = extended(jnp.concatenate([gas_state, sound_sq[None]]), depth)
    wide_state, wide_sound = wide[:4], wide[4]
    for timestep in range(STEPS):
        running = taylor(wide_state, wide_sound, depth, cells, row_count)
        last = timestep == STEPS - 1
        state = remap(running, offsets, 0 if last else depth)
        if not last:
            wide_state = radial_halos(state, depth)
    return state


def solution(mesh):
    in_specs = (P(None, None, "azi", "rad"), P(None, "azi", "rad"), P("rad"))
    out_specs = P(None, None, "azi", "rad")
    return jax.shard_map(
        per_device, mesh=mesh, in_specs=in_specs, out_specs=out_specs, check_vma=False
    )
```

```python
import functools

import jax
import jax.numpy as jnp
from jax import lax
from jax.sharding import PartitionSpec as P
from jax.experimental import pallas as pl
from jax.experimental.pallas import tpu as pltpu

ORDER = 4
STEPS = 2


TIME_STEP = 0.5
ANGULAR_RATE = 1.0
SHEAR_RATE = 1.5


def ring(axis, by):
    count = lax.axis_size(axis)
    return [(i, (i + by) % count) for i in range(count)]


def window(values, start, length, which_dim):
    return lax.slice_in_dim(values, start, start + length, axis=which_dim)


def diff_along(values, which_dim):
    length = values.shape[which_dim] - 4
    return (
        8.0 * (window(values, 3, length, which_dim) - window(values, 1, length, which_dim))
        - (window(values, 4, length, which_dim) - window(values, 0, length, which_dim))
    ) / 12.0


def diff_vertical(values):
    return (
        8.0 * (jnp.roll(values, -1, 0) - jnp.roll(values, 1, 0))
        - (jnp.roll(values, -2, 0) - jnp.roll(values, 2, 0))
    ) / 12.0


def azimuthal_halos(cells, depth):
    count = cells.shape[2]
    return jnp.concatenate(
        [
            lax.ppermute(cells[:, :, count - depth:, :], "azi", ring("azi", 1)),
            cells,
            lax.ppermute(cells[:, :, :depth, :], "azi", ring("azi", -1)),
        ],
        axis=2,
    )


def radial_halos(cells, depth):
    rows = cells.shape[3]
    low = jnp.swapaxes(cells[..., rows - depth:], 2, 3)
    high = jnp.swapaxes(cells[..., :depth], 2, 3)
    low = jnp.swapaxes(lax.ppermute(low, "rad", ring("rad", 1)), 2, 3)
    high = jnp.swapaxes(lax.ppermute(high, "rad", ring("rad", -1)), 2, 3)
    lanes = 128 * -(-(rows + 2 * depth) // 128)
    unused = jnp.zeros(cells.shape[:3] + (lanes - rows - 2 * depth,), cells.dtype)
    return jnp.concatenate([cells, high, unused, low], axis=3)


def extended(cells, depth):
    return radial_halos(azimuthal_halos(cells, depth), depth)


def inside_rows(lanes, depth, row_count):
    lane = jnp.arange(lanes, dtype=jnp.int32)
    lane = jnp.where(lane >= lanes - depth, lane - lanes, lane)
    global_row = lax.axis_index("rad") * row_count + lane
    return (global_row >= 0) & (global_row < row_count * lax.axis_size("rad"))


def operator_core(pressure, radial_flow, azimuth_flow, vertical_flow):
    density_rate = -(
        diff_along(radial_flow[:, 2:-2, :], 2)
        + diff_along(azimuth_flow[:, :, 2:-2], 1)
        + diff_vertical(inner_part(vertical_flow))
    )
    radial_rate = -diff_along(pressure[:, 2:-2, :], 2) + 2.0 * ANGULAR_RATE * inner_part(
        azimuth_flow
    )
    azimuth_rate = -diff_along(pressure[:, :, 2:-2], 1) - (
        2.0 - SHEAR_RATE
    ) * ANGULAR_RATE * inner_part(radial_flow)
    vertical_rate = -diff_vertical(inner_part(pressure))
    return jnp.stack([density_rate, radial_rate, azimuth_rate, vertical_rate])


def inner_part(values):
    return values[:, 2:-2, 2:-2]


def lane_diff(values):
    size = values.shape[1]
    return (
        8.0 * (pltpu.roll(values, size - 1, 1) - pltpu.roll(values, 1, 1))
        - (pltpu.roll(values, size - 2, 1) - pltpu.roll(values, 2, 1))
    ) / 12.0


def sublane_diff(values):
    size = values.shape[0]
    return (
        8.0 * (pltpu.roll(values, size - 1, 0) - pltpu.roll(values, 1, 0))
        - (pltpu.roll(values, size - 2, 0) - pltpu.roll(values, 2, 0))
    ) / 12.0


def taylor_kernel(keep_ref, sound_ref, state_ref, running_ref, even_ref, odd_ref, own):
    keep = keep_ref[...] != 0.0
    levels = state_ref.shape[1]
    first, cells, rows = own

    def start(level, carry):
        for field in range(4):
            values = state_ref[field, level]
            running_ref[field, level] = values[first:first + cells, :rows]
            even_ref[field, level] = jnp.where(keep, values, 0.0)
        even_ref[4, level] = sound_ref[level] * even_ref[0, level]
        return carry

    lax.fori_loop(0, levels, start, 0)
    for degree in range(1, ORDER + 1):
        source, target = (even_ref, odd_ref) if degree % 2 else (odd_ref, even_ref)
        last = degree == ORDER
        region = (slice(first, first + cells), slice(0, rows)) if last else (slice(None), slice(None))

        def order(level, carry, source=source, target=target, scale=TIME_STEP / degree,
                  last=last, region=region):
            near = [lax.rem(level + step + levels, levels) for step in (1, -1, 2, -2)]

            def vertical(value_at):
                up1, down1, up2, down2 = (value_at(at) for at in near)
                return (8.0 * (up1 - down1) - (up2 - down2)) / 12.0

            radial_flow = source[1, level]
            azimuth_flow = source[2, level]
            pressure = source[4, level]
            density_rate = -(
                lane_diff(radial_flow)[region]
                + sublane_diff(azimuth_flow)[region]
                + vertical(lambda at: source[3, at][region])
            )
            radial_rate = -lane_diff(pressure)[region] + 2.0 * ANGULAR_RATE * azimuth_flow[region]
            azimuth_rate = -sublane_diff(pressure)[region] - (
                2.0 - SHEAR_RATE
            ) * ANGULAR_RATE * radial_flow[region]
            vertical_rate = -vertical(lambda at: source[4, at][region])
            rates = (density_rate, radial_rate, azimuth_rate, vertical_rate)
            inside = keep[:, region[1]]
            for field, rate in enumerate(rates):
                series = jnp.where(inside, scale * rate, 0.0)
                if not last:
                    target[field, level] = series
                    if field == 0:
                        target[4, level] = sound_ref[level] * series
                own_part = series if last else series[first:first + cells, :rows]
                running_ref[field, level] = running_ref[field, level] + own_part
            return carry

        lax.fori_loop(0, levels, order, 0)


def taylor(wide_state, wide_sound, depth, cells, row_count):
    keep = inside_rows(wide_state.shape[3], depth, row_count).astype(jnp.float32)[None, :]
    whole = pl.BlockSpec(memory_space=pltpu.VMEM)
    size = wide_state.size
    running = pl.pallas_call(
        functools.partial(taylor_kernel, own=(depth, cells, row_count)),
        out_shape=jax.ShapeDtypeStruct(wide_state.shape[:2] + (cells, row_count), jnp.float32),
        in_specs=[whole, whole, whole],
        out_specs=whole,
        scratch_shapes=[pltpu.VMEM((5,) + wide_state.shape[1:], jnp.float32)] * 2,
        compiler_params=pltpu.CompilerParams(vmem_limit_bytes=48 * 1024 * 1024),
        cost_estimate=pl.CostEstimate(
            flops=60 * ORDER * size, transcendentals=0, bytes_accessed=4 * (2 * size + size // 4)
        ),
    )(keep, wide_sound, wide_state)
    return running


def roll_cells(blocks, shift):
    cells = blocks.shape[2]
    whole, part = divmod(shift, cells)
    if whole:
        blocks = jnp.roll(blocks, whole, axis=0)
    if part:
        carried = jnp.roll(blocks, 1, axis=0)
        blocks = jnp.concatenate(
            [carried[:, :, cells - part:], blocks[:, :, :cells - part]], axis=2
        )
    return blocks


def remap(state, offsets, depth):
    fields, levels, cells, rows = state.shape
    peers = lax.axis_size("azi")
    planes = state.reshape(peers, fields * levels // peers, cells, rows)
    blocks = lax.all_to_all(planes, "azi", 0, 0, tiled=True)
    total = peers * cells
    for bit_pos in range((total - 1).bit_length()):
        chosen = (offsets >> bit_pos) & 1 == 1
        blocks = jnp.where(chosen, roll_cells(blocks, 1 << bit_pos), blocks)
    if depth:
        blocks = jnp.concatenate(
            [jnp.roll(blocks, 1, axis=0)[:, :, cells - depth:], blocks,
             jnp.roll(blocks, -1, axis=0)[:, :, :depth]],
            axis=2,
        )
    planes = lax.all_to_all(blocks, "azi", 0, 0, tiled=True)
    return planes.reshape(fields, levels, cells + 2 * depth, rows)


def per_device(gas_state, sound_sq, offsets):
    depth = 2 * ORDER
    cells, row_count = gas_state.shape[2], gas_state.shape[3]
    wide = extended(jnp.concatenate([gas_state, sound_sq[None]]), depth)
    wide_state, wide_sound = wide[:4], wide[4]
    for timestep in range(STEPS):
        running = taylor(wide_state, wide_sound, depth, cells, row_count)
        last = timestep == STEPS - 1
        state = remap(running, offsets, 0 if last else depth)
        if not last:
            wide_state = radial_halos(state, depth)
    return state


def solution(mesh):
    in_specs = (P(None, None, "azi", "rad"), P(None, "azi", "rad"), P("rad"))
    out_specs = P(None, None, "azi", "rad")
    return jax.shard_map(
        per_device, mesh=mesh, in_specs=in_specs, out_specs=out_specs, check_vma=False
    )
```
